128 devices in a mesh: region: 8 (over y, core), node: 16 (over x, z).
Axes of the slice: x: 4, y: 4, z: 4, core: 2. Of those that a mesh axis runs over, the one named last changes fastest.
Arguments:
- impedance: float32 [16, 4096, 4096], P('region', 'node'), as said below
- source_amp: float32 [16, 64, 4096], P('region', None, 'node'), may hold values from -6 to 6
- source_angle: float32 [16, 4096], P('region', 'node'), may hold values from -3.140625 to 3.140625
- impulse_taps: float32 [512, 131072], P(None, ('region', 'node'))
- incident: float32 [515, 131072], P(None, ('region', 'node')), may hold values from -6 to 6
- conductance: float32 [131072], P(('region', 'node')), may hold values from 0.5 to 2
- attach: int32 [131072], P(('region', 'node')), may hold values from 0 to 511
- pair_slot: int32 [128, 1024], P(('region', 'node')), may hold values from 0 to 1024, as said below
- fault_node: int32 [16, 64], P('region'), may hold values from 0 to 4095
- fault_step: int32 [16, 64], P('region'), may hold values from 0 to 7
- fault_res: float32 [16, 64], P('region'), may hold values from 0.1 to 1
Outputs:
- voltages: float32 [8, 16, 64, 4096], P(None, 'region', None, 'node')
The draws below stay inside these ranges and needn't reach their ends.
Inputs may be any that keep to these rules, and one draw needn't show every extreme that they name: impedance[s] is a symmetric matrix for every s. `pair_slot`: row d (d = region index * 16 + node index) holds at position e * 8 + s, for each device e and slot s, a line end of device d paired with the one named at position d * 8 + s of row e, or 1024 where that slot is empty; a slot is filled in row d exactly when its mirror in row e is filled; each line end stands in at most one slot; in every draw some device pair fills all 8 slots.
All inputs are finite; a program needn't handle non-finite values.
Results may differ from the reference program's by a relative error of at most 0.0001.
Values sent between devices are 32-bit elements; how exact they have to be, the bound alone decides.
No kernel may reach another device: no remote copies, remote signals or barrier semaphores. Data moves between devices by JAX's collectives and lax.ppermute only.
A program may use at most 128 MiB of HBM per device.

```python
import math
import jax
import jax.numpy as jnp
from jax import lax

SUB_ORDER = 4096
FAULT_CASES = 64
TAP_COUNT = 512
WINDOW_STEPS = 4
WINDOW_COUNT = 2
SUBS_REGION = 2
ENDS_DEV = 1024
SUBNETWORKS = 16
ROWS_DEV = 256
LOCAL_ROWS = 512
LINE_ENDS = 131072
PAIR_SLOTS = 8
TOTAL_STEPS = 8
PAST_STEPS = 515
N_NODE = 16


def draw_impedance(key, part):
    subkeys = jax.random.split(key, SUBNETWORKS)

    def one_matrix(subkey):
        first_key, second_key = jax.random.split(subkey)
        entries = jax.random.truncated_normal(first_key, -3.0, 3.0, (SUB_ORDER, SUB_ORDER), jnp.float32)
        diagonal = jnp.exp(jax.random.uniform(second_key, (SUB_ORDER,), jnp.float32, math.log(0.5), math.log(2.0)))
        mixed = (entries + entries.T) * (0.7071 / math.sqrt(SUB_ORDER))
        row_ids = lax.iota(jnp.int32, SUB_ORDER)
        on_diag = row_ids[:, None] == row_ids[None, :]
        return jnp.where(on_diag, mixed + diagonal[:, None], mixed)
    return lax.map(one_matrix, subkeys)


def draw_impulse_taps(key, part):
    first_key, second_key = jax.random.split(key)
    lag_values = lax.iota(jnp.float32, TAP_COUNT)[:, None]
    decay_time = jnp.exp(jax.random.uniform(first_key, (1, LINE_ENDS), jnp.float32, math.log(4.0), math.log(TAP_COUNT)))
    noise = jax.random.normal(second_key, (TAP_COUNT, LINE_ENDS), jnp.float32)
    return 0.6 * noise * jnp.exp(-lag_values / decay_time) / jnp.sqrt(decay_time)


def draw_pair_slot(key, part):
    peers = LINE_ENDS // ENDS_DEV
    key_one, key_two, key_three, key_four = jax.random.split(key, 4)
    counts = jax.random.randint(key_one, (peers, peers), 0, PAIR_SLOTS + 1)
    row_ids = lax.iota(jnp.int32, peers)[:, None]
    col_ids = lax.iota(jnp.int32, peers)[None, :]
    counts = jnp.where(row_ids <= col_ids, counts, counts.T)
    first = jax.random.randint(key_two, (), 0, peers)
    second = jax.random.randint(key_three, (), 0, peers)
    forced = (row_ids == first) & (col_ids == second) | (row_ids == second) & (col_ids == first)
    counts = jnp.where(forced, PAIR_SLOTS, counts)
    slot_pos = lax.iota(jnp.int32, PAIR_SLOTS)[None, None, :]
    live = (slot_pos < counts[:, :, None]).reshape(peers, ENDS_DEV).astype(jnp.int32)
    ranks = jnp.cumsum(live, axis=1) - live

    def pick_order(subkey):
        return jax.random.permutation(subkey, ENDS_DEV).astype(jnp.int32)
    orders = jax.vmap(pick_order)(jax.random.split(key_four, peers))
    chosen = jnp.take_along_axis(orders, ranks, axis=1)
    return jnp.where(live == 1, chosen, ENDS_DEV).astype(jnp.int32)


def place_ends(array, own_key, low, top_value):
    longest = array.shape.index(max(array.shape))
    spots = []
    for shift in (0, 1):
        where = [jax.random.randint(jax.random.fold_in(own_key, axis), (), 0, length) for axis, length in enumerate(array.shape)]
        where[longest] = (where[longest] + shift) % array.shape[longest]
        spots.append(tuple(where))
    return array.at[spots[0]].set(low).at[spots[1]].set(top_value)


def block_levels(stream_key, dims, pieces, smallest, top_value):
    factor_of = 1.0
    for axis_at, parts in pieces:
        steps = jax.random.uniform(jax.random.fold_in(jax.random.fold_in(stream_key, 6), axis_at), (parts,), jnp.float32, smallest / len(pieces), top_value / len(pieces))
        factor_of = factor_of * jnp.repeat(jnp.exp(steps), dims[axis_at] // parts).reshape((-1,) + (1,) * (len(dims) - 1 - axis_at))
    return factor_of


def normal_values(rng, dims, deviation, most, shards=(), kind=jnp.bfloat16):
    array = jax.random.normal(rng, dims, jnp.float32) * deviation
    if len(shards) > 0:
        array = block_levels(rng, dims, shards, -0.22, 0.18) * array
    return jnp.clip(array, min=-most, max=most).astype(kind)


def setup_inputs(seed: int = 0) -> dict:
    key_list = jax.random.split(jax.random.key(seed), 12)
    impedance = draw_impedance(jax.random.fold_in(key_list[11], 71), 0)
    source_amp = normal_values(key_list[1], (SUBNETWORKS, FAULT_CASES, SUB_ORDER), 1.0, 6.0, ((0, 8), (2, 16)), jnp.float32)
    source_angle = jnp.clip(jax.random.uniform(key_list[2], (SUBNETWORKS, SUB_ORDER), jnp.float32, -3.140625, 3.140625), -3.140625, 3.140625)
    impulse_taps = draw_impulse_taps(jax.random.fold_in(key_list[11], 71), 0)
    incident = normal_values(key_list[4], (PAST_STEPS, LINE_ENDS), 1.0, 6.0, ((1, 128),), jnp.float32)
    conductance = jnp.clip(jnp.exp(math.log(2.0) - 1.3862944 * jax.random.uniform(key_list[5], (LINE_ENDS,), jnp.float32) ** block_levels(key_list[5], (LINE_ENDS,), ((0, 128),), -0.2, 0.2)), 0.5, 2.0)
    attach = place_ends(jax.random.randint(key_list[6], (LINE_ENDS,), 0, LOCAL_ROWS), jax.random.fold_in(key_list[6], 1), 0, LOCAL_ROWS - 1).astype(jnp.int32)
    pair_slot = draw_pair_slot(jax.random.fold_in(key_list[11], 71), 0)
    fault_node = place_ends(jax.random.randint(key_list[8], (SUBNETWORKS, FAULT_CASES), 0, SUB_ORDER), jax.random.fold_in(key_list[8], 1), 0, SUB_ORDER - 1).astype(jnp.int32)
    fault_step = place_ends(jax.random.randint(key_list[9], (SUBNETWORKS, FAULT_CASES), 0, TOTAL_STEPS), jax.random.fold_in(key_list[9], 1), 0, TOTAL_STEPS - 1).astype(jnp.int32)
    fault_res = jnp.clip(jnp.exp(math.log(1.0) - 2.3025851 * jax.random.uniform(key_list[10], (SUBNETWORKS, FAULT_CASES), jnp.float32) ** block_levels(key_list[10], (SUBNETWORKS, FAULT_CASES), ((0, 8),), -0.2, 0.2)), 0.1, 1.0)
    return dict(impedance=impedance, source_amp=source_amp, source_angle=source_angle, impulse_taps=impulse_taps, incident=incident, conductance=conductance, attach=attach, pair_slot=pair_slot, fault_node=fault_node, fault_step=fault_step, fault_res=fault_res)


omega_step = 2.0 * math.pi / 400.0


def reference(impedance, source_amp, source_angle, impulse_taps, incident, conductance, attach, pair_slot, fault_node, fault_step, fault_res):
    precise = lax.Precision.HIGHEST
    end_ids = jnp.arange(LINE_ENDS, dtype=jnp.int32)
    device = end_ids // ENDS_DEV
    subnet_of = (device // N_NODE) * SUBS_REGION + attach // ROWS_DEV
    row_of = (device % N_NODE) * ROWS_DEV + attach % ROWS_DEV
    flat_node = (subnet_of * SUB_ORDER + row_of).astype(jnp.int32)
    peers = LINE_ENDS // ENDS_DEV
    dev_grid = jnp.arange(peers, dtype=jnp.int32)[:, None]
    slot_grid = jnp.arange(ENDS_DEV, dtype=jnp.int32)[None, :]
    peer_grid = slot_grid // PAIR_SLOTS
    within = slot_grid % PAIR_SLOTS
    mirror = pair_slot[peer_grid, dev_grid * PAIR_SLOTS + within]
    valid = pair_slot < ENDS_DEV
    target = jnp.where(valid, dev_grid * ENDS_DEV + pair_slot, LINE_ENDS).reshape(-1).astype(jnp.int32)
    source_end = jnp.where(valid, peer_grid * ENDS_DEV + mirror, 0).reshape(-1).astype(jnp.int32)
    partner = jnp.zeros((LINE_ENDS,), jnp.int32).at[target].set(source_end, mode="drop")
    paired = jnp.zeros((LINE_ENDS,), jnp.int32).at[target].set(1, mode="drop") > 0
    column_index = jnp.broadcast_to(fault_node[:, None, :], (SUBNETWORKS, SUB_ORDER, FAULT_CASES))
    fault_column = jnp.transpose(jnp.take_along_axis(impedance, column_index, axis=2), (0, 2, 1))
    fault_self = jnp.take_along_axis(fault_column, fault_node[:, :, None], axis=2)[:, :, 0]
    step_total = WINDOW_STEPS * WINDOW_COUNT
    padded = jnp.concatenate([incident, jnp.zeros((step_total - WINDOW_STEPS, LINE_ENDS), jnp.float32)], axis=0)
    flipped = impulse_taps[::-1]
    base = [jnp.sum(flipped * padded[instant:instant + TAP_COUNT], axis=0) for instant in range(step_total)]
    far_list = []
    results = []
    for instant in range(step_total):
        history = jnp.broadcast_to(base[instant][None, :], (FAULT_CASES, LINE_ENDS))
        for delay_index in range(instant - WINDOW_STEPS + 1):
            history = history + impulse_taps[delay_index][None, :] * far_list[instant - WINDOW_STEPS - delay_index]
        node_hist = jax.ops.segment_sum(history.T, flat_node, num_segments=SUBNETWORKS * SUB_ORDER)
        node_hist = jnp.transpose(node_hist.reshape(SUBNETWORKS, SUB_ORDER, FAULT_CASES), (0, 2, 1))
        phase_now = jnp.cos(omega_step * instant + source_angle)
        injection = source_amp * phase_now[:, None, :] + node_hist
        open_volts = jnp.einsum("sij,scj->sci", impedance, injection, precision=precise)
        at_fault = jnp.take_along_axis(open_volts, fault_node[:, :, None], axis=2)[:, :, 0]
        current = jnp.where(fault_step <= instant, at_fault / (fault_self + fault_res), 0.0)
        voltage = open_volts - current[:, :, None] * fault_column
        results.append(voltage)
        at_ends = jnp.transpose(voltage, (1, 0, 2)).reshape(FAULT_CASES, SUBNETWORKS * SUB_ORDER)[:, flat_node]
        wave = 2.0 * conductance[None, :] * at_ends - history
        far_list.append(jnp.where(paired[None, :], wave[:, partner], 0.0))
    return jnp.stack(results)
```

```python
import math

import jax
import jax.numpy as jnp
from jax import lax
from jax.sharding import PartitionSpec as P

WINDOW_STEPS = 4
WINDOW_COUNT = 2


omega_step = 2.0 * math.pi / 400.0
PRECISE = lax.Precision.HIGHEST


def mm(spec, a, b):
    return jnp.einsum(spec, a, b, precision=PRECISE, preferred_element_type=jnp.float32)


def body(
    impedance,
    source_amp,
    source_angle,
    impulse_taps,
    incident,
    conductance,
    attach,
    pair_slot,
    fault_node,
    fault_step,
    fault_res,
):
    subnets, rows, order = impedance.shape
    cases = source_amp.shape[1]
    tap_len, ends = impulse_taps.shape
    past = incident.shape[0]
    steps = WINDOW_STEPS
    total = WINDOW_STEPS * WINDOW_COUNT
    n_node = order // rows
    row_ids = lax.axis_index("node") * rows + lax.iota(jnp.int32, rows)

    attach_map = (attach[:, None] == lax.iota(jnp.int32, subnets * rows)[None, :]).astype(jnp.float32)

    index = jnp.broadcast_to(fault_node[:, None, :], (subnets, rows, cases))
    fault_col = jnp.take_along_axis(impedance, index, axis=2)
    fault_colT = jnp.transpose(fault_col, (0, 2, 1))
    owner = (fault_node[:, :, None] == row_ids[None, None, :]).astype(jnp.float32)
    self_part = jnp.sum(fault_colT * owner, axis=2)

    flip = (lax.iota(jnp.int32, tap_len)[:, None] + lax.iota(jnp.int32, tap_len)[None, :] == tap_len - 1).astype(
        jnp.float32
    )
    taps_rev = mm("uj,jk->uk", flip, impulse_taps)
    padded = jnp.concatenate([incident, jnp.zeros((tap_len + total - 1 - past, ends), jnp.float32)], axis=0)
    base = jnp.stack([jnp.sum(taps_rev * padded[t : t + tap_len], axis=0) for t in range(total)])
    base_node = mm("tk,kr->tr", base, attach_map).reshape(total, subnets, rows)

    amp_cos = source_amp * jnp.cos(source_angle)[:, None, :]
    amp_sin = source_amp * jnp.sin(source_angle)[:, None, :]
    h0 = jnp.transpose(base_node[:steps], (1, 0, 2))
    part_cos = jnp.sum(fault_colT * amp_cos, axis=2)
    part_sin = jnp.sum(fault_colT * amp_sin, axis=2)
    part_h = mm("sci,sti->stc", fault_colT, h0)
    partials = jnp.concatenate(
        [part_cos[:, None], part_sin[:, None], part_h, self_part[:, None]], axis=1
    ).reshape(subnets, -1)
    pad_len = 2 * rows - partials.shape[1]
    partials = jnp.concatenate([partials, jnp.zeros((subnets, pad_len), jnp.float32)], axis=1)
    payload = jnp.concatenate(
        [amp_cos, amp_sin, h0, partials.reshape(subnets, 2, rows), jnp.zeros((subnets, 2, rows), jnp.float32)],
        axis=1,
    )
    gathered = lax.all_gather(payload, "node", axis=2, tiled=True)
    lead = 2 * cases + steps
    prod = mm("srj,scj->scr", impedance, gathered[:, :lead])
    sums = jnp.sum(gathered[:, lead : lead + 2].reshape(subnets, 2, n_node, rows), axis=2).reshape(subnets, 2 * rows)
    sums = sums[:, : 7 * cases].reshape(subnets, 7, cases)
    fault_self = sums[:, 6]
    denominator = fault_self + fault_res

    results = []
    waves = []
    for t in range(steps):
        cw = math.cos(omega_step * t)
        sw = math.sin(omega_step * t)
        open_v = cw * prod[:, :cases] - sw * prod[:, cases : 2 * cases] + prod[:, 2 * cases + t][:, None, :]
        at_fault = cw * sums[:, 0] - sw * sums[:, 1] + sums[:, 2 + t]
        current = jnp.where(fault_step <= t, at_fault / denominator, 0.0)
        voltage = open_v - current[:, :, None] * fault_colT
        results.append(voltage)
        at_ends = mm("sci,ksi->ck", voltage, attach_map.reshape(ends, subnets, rows))
        waves.append(2.0 * conductance[None, :] * at_ends - base[t][None, :])

    slot_row = pair_slot[0]
    end_ids = lax.iota(jnp.int32, ends)
    selector = (end_ids[:, None] == slot_row[None, :]).astype(jnp.float32)
    wave_block = jnp.stack(waves).reshape(steps * cases, ends)
    outgoing = mm("kp,mk->pm", selector, wave_block)
    incoming = lax.all_to_all(outgoing, ("region", "node"), 0, 0, tiled=True)
    far = mm("pm,kp->mk", incoming, selector).reshape(steps, cases, ends)

    inj_list = []
    for t in range(steps, total):
        history = base[t][None, :]
        for j in range(t - steps + 1):
            history = history + impulse_taps[j][None, :] * far[t - steps - j]
        node_hist = mm("ck,ksi->sci", history, attach_map.reshape(ends, subnets, rows))
        phase = jnp.cos(omega_step * t + source_angle)
        inj_list.append(source_amp * phase[:, None, :] + node_hist)
    inj1 = jnp.stack(inj_list, axis=1)
    part1 = jnp.sum(fault_colT[:, None] * inj1, axis=3).reshape(subnets, 1, steps * cases)
    part1 = jnp.concatenate(
        [part1.reshape(subnets, -1, rows), jnp.zeros((subnets, 8 - steps * cases // rows, rows), jnp.float32)], axis=1
    )
    payload1 = jnp.concatenate([inj1.reshape(subnets, steps * cases, rows), part1], axis=1)
    gathered1 = lax.all_gather(payload1, "node", axis=2, tiled=True)
    body_rows = steps * cases
    prod1 = mm("srj,scj->scr", impedance, gathered1[:, :body_rows]).reshape(subnets, steps, cases, rows)
    part_rows = steps * cases // rows
    sums1 = jnp.sum(
        gathered1[:, body_rows : body_rows + part_rows].reshape(subnets, part_rows, n_node, rows), axis=2
    ).reshape(subnets, steps, cases)
    for t in range(steps, total):
        open_v = prod1[:, t - steps]
        current = jnp.where(fault_step <= t, sums1[:, t - steps] / denominator, 0.0)
        results.append(open_v - current[:, :, None] * fault_colT)
    return jnp.stack(results)


def solution(mesh):
    in_specs = (
        P("region", "node", None),
        P("region", None, "node"),
        P("region", "node"),
        P(None, ("region", "node")),
        P(None, ("region", "node")),
        P(("region", "node")),
        P(("region", "node")),
        P(("region", "node"), None),
        P("region", None),
        P("region", None),
        P("region", None),
    )
    out_specs = P(None, "region", None, "node")
    return jax.shard_map(body, mesh=mesh, in_specs=in_specs, out_specs=out_specs, check_vma=False)
```

```python
import math

import jax
import jax.numpy as jnp
from jax import lax
from jax.sharding import PartitionSpec as P

WINDOW_STEPS = 4
WINDOW_COUNT = 2


omega_step = 2.0 * math.pi / 400.0
PRECISE = lax.Precision.HIGHEST


def mm(spec, a, b):
    return jnp.einsum(spec, a, b, precision=PRECISE, preferred_element_type=jnp.float32)


def body(
    impedance,
    source_amp,
    source_angle,
    impulse_taps,
    incident,
    conductance,
    attach,
    pair_slot,
    fault_node,
    fault_step,
    fault_res,
):
    subnets, rows, order = impedance.shape
    cases = source_amp.shape[1]
    tap_len, ends = impulse_taps.shape
    past = incident.shape[0]
    steps = WINDOW_STEPS
    total = WINDOW_STEPS * WINDOW_COUNT
    n_node = order // rows
    row_ids = lax.axis_index("node") * rows + lax.iota(jnp.int32, rows)

    attach_map = (attach[:, None] == lax.iota(jnp.int32, subnets * rows)[None, :]).astype(jnp.float32)

    onehot = (fault_node[:, :, None] == lax.iota(jnp.int32, order)[None, None, :]).astype(jnp.float32)
    fault_colT = mm("srj,scj->scr", impedance, onehot)
    owner = (fault_node[:, :, None] == row_ids[None, None, :]).astype(jnp.float32)
    self_part = jnp.sum(fault_colT * owner, axis=2)

    flip = (lax.iota(jnp.int32, tap_len)[:, None] + lax.iota(jnp.int32, tap_len)[None, :] == tap_len - 1).astype(
        jnp.float32
    )
    taps_rev = mm("uj,jk->uk", flip, impulse_taps)
    padded = jnp.concatenate([incident, jnp.zeros((tap_len + total - 1 - past, ends), jnp.float32)], axis=0)
    base = jnp.stack([jnp.sum(taps_rev * padded[t : t + tap_len], axis=0) for t in range(total)])
    base_node = mm("tk,kr->tr", base, attach_map).reshape(total, subnets, rows)

    amp_cos = source_amp * jnp.cos(source_angle)[:, None, :]
    amp_sin = source_amp * jnp.sin(source_angle)[:, None, :]
    sources = lax.all_gather(jnp.concatenate([amp_cos, amp_sin], axis=1), "node", axis=2, tiled=True)
    h0 = jnp.transpose(base_node[:steps], (1, 0, 2))
    part_cos = jnp.sum(fault_colT * amp_cos, axis=2)
    part_sin = jnp.sum(fault_colT * amp_sin, axis=2)
    part_h = mm("sci,sti->stc", fault_colT, h0)
    partials = jnp.concatenate(
        [part_cos[:, None], part_sin[:, None], part_h, self_part[:, None]], axis=1
    ).reshape(subnets, -1)
    pad_len = 2 * rows - partials.shape[1]
    partials = jnp.concatenate([partials, jnp.zeros((subnets, pad_len), jnp.float32)], axis=1)
    small = jnp.concatenate([h0, partials.reshape(subnets, 2, rows)], axis=1)
    small = jnp.broadcast_to(small[None], (n_node,) + small.shape)
    small = lax.all_to_all(small, "node", 0, 0, tiled=True)
    h0_full = jnp.transpose(small[:, :, :steps], (1, 2, 0, 3)).reshape(subnets, steps, order)
    prod = mm("srj,scj->scr", impedance, jnp.concatenate([sources, h0_full], axis=1))
    sums = jnp.sum(small[:, :, steps:], axis=0).reshape(subnets, 2 * rows)
    sums = sums[:, : 7 * cases].reshape(subnets, 7, cases)
    fault_self = sums[:, 6]
    denominator = fault_self + fault_res

    results = []
    waves = []
    for t in range(steps):
        cw = math.cos(omega_step * t)
        sw = math.sin(omega_step * t)
        open_v = cw * prod[:, :cases] - sw * prod[:, cases : 2 * cases] + prod[:, 2 * cases + t][:, None, :]
        at_fault = cw * sums[:, 0] - sw * sums[:, 1] + sums[:, 2 + t]
        current = jnp.where(fault_step <= t, at_fault / denominator, 0.0)
        voltage = open_v - current[:, :, None] * fault_colT
        results.append(voltage)
        at_ends = mm("sci,ksi->ck", voltage, attach_map.reshape(ends, subnets, rows))
        waves.append(2.0 * conductance[None, :] * at_ends - base[t][None, :])

    slot_row = pair_slot[0]
    end_ids = lax.iota(jnp.int32, ends)
    selector = (end_ids[:, None] == slot_row[None, :]).astype(jnp.float32)
    wave_block = jnp.stack(waves).reshape(steps * cases, ends)
    outgoing = mm("kp,mk->pm", selector, wave_block)
    incoming = lax.all_to_all(outgoing, ("region", "node"), 0, 0, tiled=True)
    far = mm("pm,kp->mk", incoming, selector).reshape(steps, cases, ends)

    inj_list = []
    for t in range(steps, total):
        history = base[t][None, :]
        for j in range(t - steps + 1):
            history = history + impulse_taps[j][None, :] * far[t - steps - j]
        node_hist = mm("ck,ksi->sci", history, attach_map.reshape(ends, subnets, rows))
        phase = jnp.cos(omega_step * t + source_angle)
        inj_list.append(source_amp * phase[:, None, :] + node_hist)
    inj1 = jnp.stack(inj_list, axis=1)
    part1 = jnp.sum(fault_colT[:, None] * inj1, axis=3).reshape(subnets, 1, steps * cases)
    part1 = jnp.concatenate(
        [part1.reshape(subnets, -1, rows), jnp.zeros((subnets, 8 - steps * cases // rows, rows), jnp.float32)], axis=1
    )
    payload1 = jnp.concatenate([inj1.reshape(subnets, steps * cases, rows), part1], axis=1)
    gathered1 = lax.all_gather(payload1, "node", axis=2, tiled=True)
    body_rows = steps * cases
    prod1 = mm("srj,scj->scr", impedance, gathered1[:, :body_rows]).reshape(subnets, steps, cases, rows)
    part_rows = steps * cases // rows
    sums1 = jnp.sum(
        gathered1[:, body_rows : body_rows + part_rows].reshape(subnets, part_rows, n_node, rows), axis=2
    ).reshape(subnets, steps, cases)
    for t in range(steps, total):
        open_v = prod1[:, t - steps]
        current = jnp.where(fault_step <= t, sums1[:, t - steps] / denominator, 0.0)
        results.append(open_v - current[:, :, None] * fault_colT)
    return jnp.stack(results)


def solution(mesh):
    in_specs = (
        P("region", "node", None),
        P("region", None, "node"),
        P("region", "node"),
        P(None, ("region", "node")),
        P(None, ("region", "node")),
        P(("region", "node")),
        P(("region", "node")),
        P(("region", "node"), None),
        P("region", None),
        P("region", None),
        P("region", None),
    )
    out_specs = P(None, "region", None, "node")
    return jax.shard_map(body, mesh=mesh, in_specs=in_specs, out_specs=out_specs, check_vma=False)
```

```python
import math

import jax
import numpy as np
import jax.numpy as jnp
from jax import lax
from jax.sharding import PartitionSpec as P

WINDOW_STEPS = 4
WINDOW_COUNT = 2


omega_step = 2.0 * math.pi / 400.0
PRECISE = lax.Precision.HIGHEST


def mm(spec, a, b):
    return jnp.einsum(spec, a, b, precision=PRECISE, preferred_element_type=jnp.float32)


def fast(spec, a, b):
    return jnp.einsum(spec, a, b, precision=lax.Precision.HIGH, preferred_element_type=jnp.float32)


def body(
    impedance,
    source_amp,
    source_angle,
    impulse_taps,
    incident,
    conductance,
    attach,
    pair_slot,
    fault_node,
    fault_step,
    fault_res,
):
    subnets, rows, order = impedance.shape
    cases = source_amp.shape[1]
    tap_len, ends = impulse_taps.shape
    past = incident.shape[0]
    steps = WINDOW_STEPS
    total = WINDOW_STEPS * WINDOW_COUNT
    n_node = order // rows
    row_ids = lax.axis_index("node") * rows + lax.iota(jnp.int32, rows)

    attach_map = (attach[:, None] == lax.iota(jnp.int32, subnets * rows)[None, :]).astype(jnp.float32)

    onehot = (fault_node[:, :, None] == lax.iota(jnp.int32, order)[None, None, :]).astype(jnp.float32)
    fault_colT = mm("srj,scj->scr", impedance, onehot)
    owner = (fault_node[:, :, None] == row_ids[None, None, :]).astype(jnp.float32)
    self_part = jnp.sum(fault_colT * owner, axis=2)

    flip = (lax.iota(jnp.int32, tap_len)[:, None] + lax.iota(jnp.int32, tap_len)[None, :] == tap_len - 1).astype(
        jnp.float32
    )
    taps_rev = mm("uj,jk->uk", flip, impulse_taps)
    padded = jnp.concatenate([incident, jnp.zeros((tap_len + total - 1 - past, ends), jnp.float32)], axis=0)
    base = jnp.stack([jnp.sum(taps_rev * padded[t : t + tap_len], axis=0) for t in range(total)])
    base_node = mm("tk,kr->tr", base, attach_map).reshape(total, subnets, rows)

    amp_cos = source_amp * jnp.cos(source_angle)[:, None, :]
    amp_sin = source_amp * jnp.sin(source_angle)[:, None, :]
    sources = lax.all_gather(jnp.concatenate([amp_cos, amp_sin], axis=1), "node", axis=2, tiled=True)
    h0 = jnp.transpose(base_node[:steps], (1, 0, 2))
    part_cos = jnp.sum(fault_colT * amp_cos, axis=2)
    part_sin = jnp.sum(fault_colT * amp_sin, axis=2)
    part_h = mm("sci,sti->stc", fault_colT, h0)
    partials = jnp.concatenate(
        [part_cos[:, None], part_sin[:, None], part_h, self_part[:, None]], axis=1
    ).reshape(subnets, -1)
    pad_len = 2 * rows - partials.shape[1]
    partials = jnp.concatenate([partials, jnp.zeros((subnets, pad_len), jnp.float32)], axis=1)
    small = jnp.concatenate([h0, partials.reshape(subnets, 2, rows)], axis=1)
    small = jnp.broadcast_to(small[None], (n_node,) + small.shape)
    small = lax.all_to_all(small, "node", 0, 0, tiled=True)
    h0_full = jnp.transpose(small[:, :, :steps], (1, 2, 0, 3)).reshape(subnets, steps, order)
    prod = fast("srj,scj->scr", impedance, sources)
    prod_h = fast("srj,stj->str", impedance, h0_full)
    sums = jnp.sum(small[:, :, steps:], axis=0).reshape(subnets, 2 * rows)
    sums = sums[:, : 7 * cases].reshape(subnets, 7, cases)
    fault_self = sums[:, 6]
    denominator = fault_self + fault_res
    t0 = lax.iota(jnp.int32, steps)
    cw = jnp.asarray(np.cos(omega_step * np.arange(steps)), jnp.float32)
    sw = jnp.asarray(np.sin(omega_step * np.arange(steps)), jnp.float32)
    open0 = (
        cw[:, None, None, None] * prod[None, :, :cases]
        - sw[:, None, None, None] * prod[None, :, cases:]
        + jnp.transpose(prod_h, (1, 0, 2))[:, :, None, :]
    )
    fault0 = cw[:, None, None] * sums[None, :, 0] - sw[:, None, None] * sums[None, :, 1] + jnp.transpose(sums[:, 2 : 2 + steps], (1, 0, 2))
    current0 = jnp.where(fault_step[None] <= t0[:, None, None], fault0 / denominator[None], 0.0)
    volt0 = open0 - current0[..., None] * fault_colT[None]
    at_ends = mm("tsci,ksi->tck", volt0, attach_map.reshape(ends, subnets, rows))
    waves = 2.0 * conductance[None, None, :] * at_ends - base[:steps, None, :]

    slot_row = pair_slot[0]
    end_ids = lax.iota(jnp.int32, ends)
    selector = (end_ids[:, None] == slot_row[None, :]).astype(jnp.float32)
    outgoing = mm("kp,tck->ptc", selector, waves).reshape(ends, steps * cases)
    incoming = lax.all_to_all(outgoing, ("region", "node"), 0, 0, tiled=True)
    far = mm("pm,kp->mk", incoming, selector).reshape(steps, cases, ends)

    hist_list = []
    for t in range(steps, total):
        history = base[t][None, :]
        for j in range(t - steps + 1):
            history = history + impulse_taps[j][None, :] * far[t - steps - j]
        hist_list.append(history)
    node_hist = mm("tck,ksi->stci", jnp.stack(hist_list), attach_map.reshape(ends, subnets, rows))
    t1 = lax.iota(jnp.int32, steps) + steps
    angle1 = jnp.asarray(omega_step * np.arange(steps, total), jnp.float32)
    phase = jnp.cos(angle1[None, :, None] + source_angle[:, None, :])
    inj1 = source_amp[:, None] * phase[:, :, None, :] + node_hist
    part1 = jnp.sum(fault_colT[:, None] * inj1, axis=3).reshape(subnets, 1, steps * cases)
    part1 = jnp.concatenate(
        [part1.reshape(subnets, -1, rows), jnp.zeros((subnets, 8 - steps * cases // rows, rows), jnp.float32)], axis=1
    )
    payload1 = jnp.concatenate([inj1.reshape(subnets, steps * cases, rows), part1], axis=1)
    gathered1 = lax.all_gather(payload1, "node", axis=2, tiled=True)
    body_rows = steps * cases
    prod1 = fast("srj,scj->scr", impedance, gathered1[:, :body_rows]).reshape(subnets, steps, cases, rows)
    part_rows = steps * cases // rows
    sums1 = jnp.sum(
        gathered1[:, body_rows : body_rows + part_rows].reshape(subnets, part_rows, n_node, rows), axis=2
    ).reshape(subnets, steps, cases)
    current1 = jnp.where(fault_step[None] <= t1[:, None, None], jnp.transpose(sums1, (1, 0, 2)) / denominator[None], 0.0)
    volt1 = jnp.transpose(prod1, (1, 0, 2, 3)) - current1[..., None] * fault_colT[None]
    return jnp.concatenate([volt0, volt1], axis=0)


def solution(mesh):
    in_specs = (
        P("region", "node", None),
        P("region", None, "node"),
        P("region", "node"),
        P(None, ("region", "node")),
        P(None, ("region", "node")),
        P(("region", "node")),
        P(("region", "node")),
        P(("region", "node"), None),
        P("region", None),
        P("region", None),
        P("region", None),
    )
    out_specs = P(None, "region", None, "node")
    return jax.shard_map(body, mesh=mesh, in_specs=in_specs, out_specs=out_specs, check_vma=False)
```

```python
import math

import jax
import numpy as np
import jax.numpy as jnp
from jax import lax
from jax.sharding import PartitionSpec as P

WINDOW_STEPS = 4
WINDOW_COUNT = 2


omega_step = 2.0 * math.pi / 400.0
PRECISE = lax.Precision.HIGHEST


def mm(spec, a, b):
    return jnp.einsum(spec, a, b, precision=PRECISE, preferred_element_type=jnp.float32)


def fast(spec, a, b):
    return jnp.einsum(spec, a, b, precision=lax.Precision.HIGH, preferred_element_type=jnp.float32)


def body(
    impedance,
    source_amp,
    source_angle,
    impulse_taps,
    incident,
    conductance,
    attach,
    pair_slot,
    fault_node,
    fault_step,
    fault_res,
):
    subnets, rows, order = impedance.shape
    cases = source_amp.shape[1]
    tap_len, ends = impulse_taps.shape
    past = incident.shape[0]
    steps = WINDOW_STEPS
    total = WINDOW_STEPS * WINDOW_COUNT
    n_node = order // rows
    local = subnets * rows
    row_ids = lax.axis_index("node") * rows + lax.iota(jnp.int32, rows)

    amp_t = jnp.transpose(source_amp, (0, 2, 1))
    amp_cos = amp_t * jnp.cos(source_angle)[:, :, None]
    amp_sin = amp_t * jnp.sin(source_angle)[:, :, None]
    amp_cos, amp_sin = lax.optimization_barrier((amp_cos, amp_sin))
    sources = lax.all_gather(jnp.concatenate([amp_cos, amp_sin], axis=2), "node", axis=1, tiled=True)

    local_ids = lax.iota(jnp.int32, local)
    attach_map = (attach[:, None] == local_ids[None, :]).astype(jnp.float32)
    attach_mapT = (local_ids[:, None] == attach[None, :]).astype(jnp.float32)

    onehotT = (lax.iota(jnp.int32, order)[None, :, None] == fault_node[:, None, :]).astype(jnp.float32)
    fault_col = mm("srj,sjc->src", impedance, onehotT)
    owner = (row_ids[None, :, None] == fault_node[:, None, :]).astype(jnp.float32)
    self_part = jnp.sum(fault_col * owner, axis=1)

    flip = (lax.iota(jnp.int32, tap_len)[:, None] + lax.iota(jnp.int32, tap_len)[None, :] == tap_len - 1).astype(
        jnp.float32
    )
    taps_rev = mm("uj,jk->uk", flip, impulse_taps)
    padded = jnp.concatenate([incident, jnp.zeros((tap_len + total - 1 - past, ends), jnp.float32)], axis=0)
    base = jnp.stack([jnp.sum(taps_rev * padded[t : t + tap_len], axis=0) for t in range(total)])
    base_node = mm("tk,kn->tn", base[:steps], attach_map).reshape(steps, subnets, rows)
    h0 = jnp.transpose(base_node, (1, 0, 2))

    part_cos = jnp.sum(fault_col * amp_cos, axis=1)
    part_sin = jnp.sum(fault_col * amp_sin, axis=1)
    part_h = mm("sic,sti->stc", fault_col, h0)
    partials = jnp.concatenate(
        [part_cos[:, None], part_sin[:, None], part_h, self_part[:, None]], axis=1
    ).reshape(subnets, -1)
    pad_len = 2 * rows - partials.shape[1]
    partials = jnp.concatenate([partials, jnp.zeros((subnets, pad_len), jnp.float32)], axis=1)
    small = jnp.concatenate([h0, partials.reshape(subnets, 2, rows)], axis=1)
    small = jnp.broadcast_to(small[None], (n_node,) + small.shape)
    small = lax.all_to_all(small, "node", 0, 0, tiled=True)
    h0_full = jnp.transpose(small[:, :, :steps], (1, 0, 3, 2)).reshape(subnets, order, steps)
    sums = jnp.sum(small[:, :, steps:], axis=0).reshape(subnets, 2 * rows)
    sums = sums[:, : 7 * cases].reshape(subnets, 7, cases)
    denominator = sums[:, 6] + fault_res

    prod = fast("srj,sjc->src", impedance, sources)
    prod_h = fast("srj,sjt->srt", impedance, h0_full)
    t0 = lax.iota(jnp.int32, steps)
    cw = jnp.asarray(np.cos(omega_step * np.arange(steps)), jnp.float32)
    sw = jnp.asarray(np.sin(omega_step * np.arange(steps)), jnp.float32)
    open0 = (
        cw[None, None, :, None] * prod[:, :, None, :cases]
        - sw[None, None, :, None] * prod[:, :, None, cases:]
        + prod_h[:, :, :, None]
    )
    fault0 = cw[None, :, None] * sums[:, 0][:, None] - sw[None, :, None] * sums[:, 1][:, None] + sums[:, 2 : 2 + steps]
    current0 = jnp.where(fault_step[:, None, :] <= t0[None, :, None], fault0 / denominator[:, None, :], 0.0)
    volt0 = open0 - current0[:, None] * fault_col[:, :, None, :]

    at_ends = mm("kn,nm->km", attach_map, volt0.reshape(local, steps * cases)).reshape(ends, steps, cases)
    waves = 2.0 * conductance[:, None, None] * at_ends - jnp.transpose(base[:steps])[:, :, None]

    slot_row = pair_slot[0]
    end_ids = lax.iota(jnp.int32, ends)
    selector = (end_ids[:, None] == slot_row[None, :]).astype(jnp.float32)
    selectorT = (slot_row[:, None] == end_ids[None, :]).astype(jnp.float32)
    outgoing = mm("pk,km->pm", selectorT, waves.reshape(ends, steps * cases))
    incoming = lax.all_to_all(outgoing, ("region", "node"), 0, 0, tiled=True)
    far = mm("kp,pm->km", selector, incoming).reshape(ends, steps, cases)

    taps_t = jnp.transpose(impulse_taps[:steps])
    base_t = jnp.transpose(base[steps:])
    hist_list = []
    for t in range(steps, total):
        history = base_t[:, t - steps][:, None]
        for j in range(t - steps + 1):
            history = history + taps_t[:, j][:, None] * far[:, t - steps - j]
        hist_list.append(history)
    hist1 = jnp.stack(hist_list, axis=1).reshape(ends, steps * cases)
    node_hist = mm("nk,km->nm", attach_mapT, hist1).reshape(subnets, rows, steps, cases)
    angle1 = jnp.asarray(omega_step * np.arange(steps, total), jnp.float32)
    phase = jnp.cos(angle1[None, None, :] + source_angle[:, :, None])
    inj1 = amp_t[:, :, None, :] * phase[:, :, :, None] + node_hist
    part1 = jnp.sum(fault_col[:, :, None, :] * inj1, axis=1)
    part1 = lax.all_to_all(jnp.broadcast_to(part1[None], (n_node,) + part1.shape), "node", 0, 0, tiled=True)
    sums1 = jnp.sum(part1, axis=0)
    gathered1 = lax.all_gather(inj1.reshape(subnets, rows, steps * cases), "node", axis=1, tiled=True)
    prod1 = fast("srj,sjm->srm", impedance, gathered1).reshape(subnets, rows, steps, cases)
    t1 = t0 + steps
    current1 = jnp.where(fault_step[:, None, :] <= t1[None, :, None], sums1 / denominator[:, None, :], 0.0)
    volt1 = prod1 - current1[:, None] * fault_col[:, :, None, :]
    volt = jnp.concatenate([volt0, volt1], axis=2)
    return jnp.transpose(volt, (2, 0, 3, 1))


def solution(mesh):
    in_specs = (
        P("region", "node", None),
        P("region", None, "node"),
        P("region", "node"),
        P(None, ("region", "node")),
        P(None, ("region", "node")),
        P(("region", "node")),
        P(("region", "node")),
        P(("region", "node"), None),
        P("region", None),
        P("region", None),
        P("region", None),
    )
    out_specs = P(None, "region", None, "node")
    return jax.shard_map(body, mesh=mesh, in_specs=in_specs, out_specs=out_specs, check_vma=False)
```

```python
import math

import jax
import numpy as np
import jax.numpy as jnp
from jax import lax
from jax.sharding import PartitionSpec as P

WINDOW_STEPS = 4
WINDOW_COUNT = 2


omega_step = 2.0 * math.pi / 400.0
PRECISE = lax.Precision.HIGHEST


def mm(spec, a, b):
    return jnp.einsum(spec, a, b, precision=PRECISE, preferred_element_type=jnp.float32)


def split(x):
    high = x.astype(jnp.bfloat16)
    return high, (x - high.astype(jnp.float32)).astype(jnp.bfloat16)


def fast(spec, z_parts, b):
    z_high, z_low = z_parts
    b_high, b_low = split(b)

    def one(x, y):
        return jnp.einsum(spec, x, y, preferred_element_type=jnp.float32)

    return one(z_high, b_high) + one(z_high, b_low) + one(z_low, b_high)


def body(
    impedance,
    source_amp,
    source_angle,
    impulse_taps,
    incident,
    conductance,
    attach,
    pair_slot,
    fault_node,
    fault_step,
    fault_res,
):
    subnets, rows, order = impedance.shape
    cases = source_amp.shape[1]
    tap_len, ends = impulse_taps.shape
    past = incident.shape[0]
    steps = WINDOW_STEPS
    total = WINDOW_STEPS * WINDOW_COUNT
    n_node = order // rows
    local = subnets * rows
    row_ids = lax.axis_index("node") * rows + lax.iota(jnp.int32, rows)

    amp_t = jnp.transpose(source_amp, (0, 2, 1))
    amp_cos = amp_t * jnp.cos(source_angle)[:, :, None]
    amp_sin = amp_t * jnp.sin(source_angle)[:, :, None]
    amp_cos, amp_sin = lax.optimization_barrier((amp_cos, amp_sin))
    sources = lax.all_gather(jnp.concatenate([amp_cos, amp_sin], axis=2), "node", axis=1, tiled=True)

    z_parts = lax.optimization_barrier(split(impedance))

    local_ids = lax.iota(jnp.int32, local)
    attach_map = (attach[:, None] == local_ids[None, :]).astype(jnp.float32)
    attach_mapT = (local_ids[:, None] == attach[None, :]).astype(jnp.float32)

    onehotT = (lax.iota(jnp.int32, order)[None, :, None] == fault_node[:, None, :]).astype(jnp.float32)
    fault_col = mm("srj,sjc->src", impedance, onehotT)
    owner = (row_ids[None, :, None] == fault_node[:, None, :]).astype(jnp.float32)
    self_part = jnp.sum(fault_col * owner, axis=1)

    flip = (lax.iota(jnp.int32, tap_len)[:, None] + lax.iota(jnp.int32, tap_len)[None, :] == tap_len - 1).astype(
        jnp.float32
    )
    taps_rev = mm("uj,jk->uk", flip, impulse_taps)
    padded = jnp.concatenate([incident, jnp.zeros((tap_len + total - 1 - past, ends), jnp.float32)], axis=0)
    base = jnp.stack([jnp.sum(taps_rev * padded[t : t + tap_len], axis=0) for t in range(total)])
    base_node = mm("tk,kn->tn", base[:steps], attach_map).reshape(steps, subnets, rows)
    h0 = jnp.transpose(base_node, (1, 0, 2))

    part_cos = jnp.sum(fault_col * amp_cos, axis=1)
    part_sin = jnp.sum(fault_col * amp_sin, axis=1)
    part_h = mm("sic,sti->stc", fault_col, h0)
    partials = jnp.concatenate(
        [part_cos[:, None], part_sin[:, None], part_h, self_part[:, None]], axis=1
    ).reshape(subnets, -1)
    pad_len = 2 * rows - partials.shape[1]
    partials = jnp.concatenate([partials, jnp.zeros((subnets, pad_len), jnp.float32)], axis=1)
    small = jnp.concatenate([h0, partials.reshape(subnets, 2, rows)], axis=1)
    small = jnp.broadcast_to(small[None], (n_node,) + small.shape)
    small = lax.all_to_all(small, "node", 0, 0, tiled=True)
    h0_full = jnp.transpose(small[:, :, :steps], (1, 0, 3, 2)).reshape(subnets, order, steps)
    sums = jnp.sum(small[:, :, steps:], axis=0).reshape(subnets, 2 * rows)
    sums = sums[:, : 7 * cases].reshape(subnets, 7, cases)
    denominator = sums[:, 6] + fault_res

    prod = fast("srj,sjc->src", z_parts, sources)
    prod_h = fast("srj,sjt->srt", z_parts, h0_full)
    t0 = lax.iota(jnp.int32, steps)
    cw = jnp.asarray(np.cos(omega_step * np.arange(steps)), jnp.float32)
    sw = jnp.asarray(np.sin(omega_step * np.arange(steps)), jnp.float32)
    open0 = (
        cw[None, None, :, None] * prod[:, :, None, :cases]
        - sw[None, None, :, None] * prod[:, :, None, cases:]
        + prod_h[:, :, :, None]
    )
    fault0 = cw[None, :, None] * sums[:, 0][:, None] - sw[None, :, None] * sums[:, 1][:, None] + sums[:, 2 : 2 + steps]
    current0 = jnp.where(fault_step[:, None, :] <= t0[None, :, None], fault0 / denominator[:, None, :], 0.0)
    volt0 = open0 - current0[:, None] * fault_col[:, :, None, :]

    at_ends = mm("kn,nm->km", attach_map, volt0.reshape(local, steps * cases)).reshape(ends, steps, cases)
    waves = 2.0 * conductance[:, None, None] * at_ends - jnp.transpose(base[:steps])[:, :, None]

    slot_row = pair_slot[0]
    end_ids = lax.iota(jnp.int32, ends)
    selector = (end_ids[:, None] == slot_row[None, :]).astype(jnp.float32)
    selectorT = (slot_row[:, None] == end_ids[None, :]).astype(jnp.float32)
    outgoing = mm("pk,km->pm", selectorT, waves.reshape(ends, steps * cases))
    incoming = lax.all_to_all(outgoing, ("region", "node"), 0, 0, tiled=True)
    far = mm("kp,pm->km", selector, incoming).reshape(ends, steps, cases)

    taps_t = jnp.transpose(impulse_taps[:steps])
    base_t = jnp.transpose(base[steps:])
    hist_list = []
    for t in range(steps, total):
        history = base_t[:, t - steps][:, None]
        for j in range(t - steps + 1):
            history = history + taps_t[:, j][:, None] * far[:, t - steps - j]
        hist_list.append(history)
    hist1 = jnp.stack(hist_list, axis=1).reshape(ends, steps * cases)
    node_hist = mm("nk,km->nm", attach_mapT, hist1).reshape(subnets, rows, steps, cases)
    angle1 = jnp.asarray(omega_step * np.arange(steps, total), jnp.float32)
    phase = jnp.cos(angle1[None, None, :] + source_angle[:, :, None])
    inj1 = amp_t[:, :, None, :] * phase[:, :, :, None] + node_hist
    part1 = jnp.sum(fault_col[:, :, None, :] * inj1, axis=1)
    part1 = lax.all_to_all(jnp.broadcast_to(part1[None], (n_node,) + part1.shape), "node", 0, 0, tiled=True)
    sums1 = jnp.sum(part1, axis=0)
    gathered1 = lax.all_gather(inj1.reshape(subnets, rows, steps * cases), "node", axis=1, tiled=True)
    prod1 = fast("srj,sjm->srm", z_parts, gathered1).reshape(subnets, rows, steps, cases)
    t1 = t0 + steps
    current1 = jnp.where(fault_step[:, None, :] <= t1[None, :, None], sums1 / denominator[:, None, :], 0.0)
    volt1 = prod1 - current1[:, None] * fault_col[:, :, None, :]
    volt = jnp.concatenate([volt0, volt1], axis=2)
    return jnp.transpose(volt, (2, 0, 3, 1))


def solution(mesh):
    in_specs = (
        P("region", "node", None),
        P("region", None, "node"),
        P("region", "node"),
        P(None, ("region", "node")),
        P(None, ("region", "node")),
        P(("region", "node")),
        P(("region", "node")),
        P(("region", "node"), None),
        P("region", None),
        P("region", None),
        P("region", None),
    )
    out_specs = P(None, "region", None, "node")
    return jax.shard_map(body, mesh=mesh, in_specs=in_specs, out_specs=out_specs, check_vma=False)
```

```python
import math

import jax
import numpy as np
import jax.numpy as jnp
from jax import lax
from jax.sharding import PartitionSpec as P

WINDOW_STEPS = 4
WINDOW_COUNT = 2


omega_step = 2.0 * math.pi / 400.0
PRECISE = lax.Precision.HIGHEST


def mm(spec, a, b):
    return jnp.einsum(spec, a, b, precision=PRECISE, preferred_element_type=jnp.float32)


def fast(spec, a, b):
    return jnp.einsum(spec, a, b, precision=lax.Precision.HIGH, preferred_element_type=jnp.float32)


def body(
    impedance,
    source_amp,
    source_angle,
    impulse_taps,
    incident,
    conductance,
    attach,
    pair_slot,
    fault_node,
    fault_step,
    fault_res,
):
    subnets, rows, order = impedance.shape
    cases = source_amp.shape[1]
    tap_len, ends = impulse_taps.shape
    past = incident.shape[0]
    steps = WINDOW_STEPS
    total = WINDOW_STEPS * WINDOW_COUNT
    n_node = order // rows
    local = subnets * rows
    row_ids = lax.axis_index("node") * rows + lax.iota(jnp.int32, rows)

    amp_t = jnp.transpose(source_amp, (0, 2, 1))
    packed = lax.optimization_barrier(amp_t.reshape(subnets, rows // 2, 2 * cases))
    amp_full = lax.all_gather(packed, "node", axis=1, tiled=True).reshape(subnets, order, cases)
    amp_cos = amp_t * jnp.cos(source_angle)[:, :, None]
    amp_sin = amp_t * jnp.sin(source_angle)[:, :, None]

    local_ids = lax.iota(jnp.int32, local)
    attach_map = (attach[:, None] == local_ids[None, :]).astype(jnp.float32)
    attach_mapT = (local_ids[:, None] == attach[None, :]).astype(jnp.float32)

    onehotT = (lax.iota(jnp.int32, order)[None, :, None] == fault_node[:, None, :]).astype(jnp.float32)
    fault_col = mm("srj,sjc->src", impedance, onehotT)
    owner = (row_ids[None, :, None] == fault_node[:, None, :]).astype(jnp.float32)
    self_part = jnp.sum(fault_col * owner, axis=1)

    flip = (lax.iota(jnp.int32, tap_len)[:, None] + lax.iota(jnp.int32, tap_len)[None, :] == tap_len - 1).astype(
        jnp.float32
    )
    taps_rev = mm("uj,jk->uk", flip, impulse_taps)
    padded = jnp.concatenate([incident, jnp.zeros((tap_len + total - 1 - past, ends), jnp.float32)], axis=0)
    base = jnp.stack([jnp.sum(taps_rev * padded[t : t + tap_len], axis=0) for t in range(total)])
    base_node = mm("tk,kn->tn", base[:steps], attach_map).reshape(steps, subnets, rows)
    h0 = jnp.transpose(base_node, (1, 0, 2))

    part_cos = jnp.sum(fault_col * amp_cos, axis=1)
    part_sin = jnp.sum(fault_col * amp_sin, axis=1)
    part_h = mm("sic,sti->stc", fault_col, h0)
    partials = jnp.concatenate(
        [part_cos[:, None], part_sin[:, None], part_h, self_part[:, None]], axis=1
    ).reshape(subnets, -1)
    pad_len = 2 * rows - partials.shape[1]
    partials = jnp.concatenate([partials, jnp.zeros((subnets, pad_len), jnp.float32)], axis=1)
    small = jnp.concatenate(
        [h0, partials.reshape(subnets, 2, rows), source_angle[:, None], jnp.zeros((subnets, 1, rows), jnp.float32)],
        axis=1,
    )
    small = jnp.broadcast_to(small[None], (n_node,) + small.shape)
    small = lax.all_to_all(small, "node", 0, 0, tiled=True)
    h0_full = jnp.transpose(small[:, :, :steps], (1, 0, 3, 2)).reshape(subnets, order, steps)
    sums = jnp.sum(small[:, :, steps : steps + 2], axis=0).reshape(subnets, 2 * rows)
    angle_full = jnp.transpose(small[:, :, steps + 2], (1, 0, 2)).reshape(subnets, order)
    sources = jnp.concatenate(
        [amp_full * jnp.cos(angle_full)[:, :, None], amp_full * jnp.sin(angle_full)[:, :, None]], axis=2
    )
    sums = sums[:, : 7 * cases].reshape(subnets, 7, cases)
    denominator = sums[:, 6] + fault_res

    prod = fast("srj,sjc->src", impedance, sources)
    prod_h = fast("srj,sjt->srt", impedance, h0_full)
    t0 = lax.iota(jnp.int32, steps)
    cw = jnp.asarray(np.cos(omega_step * np.arange(steps)), jnp.float32)
    sw = jnp.asarray(np.sin(omega_step * np.arange(steps)), jnp.float32)
    open0 = (
        cw[None, None, :, None] * prod[:, :, None, :cases]
        - sw[None, None, :, None] * prod[:, :, None, cases:]
        + prod_h[:, :, :, None]
    )
    fault0 = cw[None, :, None] * sums[:, 0][:, None] - sw[None, :, None] * sums[:, 1][:, None] + sums[:, 2 : 2 + steps]
    current0 = jnp.where(fault_step[:, None, :] <= t0[None, :, None], fault0 / denominator[:, None, :], 0.0)
    volt0 = open0 - current0[:, None] * fault_col[:, :, None, :]

    at_ends = mm("kn,nm->km", attach_map, volt0.reshape(local, steps * cases)).reshape(ends, steps, cases)
    waves = 2.0 * conductance[:, None, None] * at_ends - jnp.transpose(base[:steps])[:, :, None]

    slot_row = pair_slot[0]
    end_ids = lax.iota(jnp.int32, ends)
    selector = (end_ids[:, None] == slot_row[None, :]).astype(jnp.float32)
    selectorT = (slot_row[:, None] == end_ids[None, :]).astype(jnp.float32)
    outgoing = mm("pk,km->pm", selectorT, waves.reshape(ends, steps * cases))
    incoming = lax.all_to_all(outgoing, ("region", "node"), 0, 0, tiled=True)
    far = mm("kp,pm->km", selector, incoming).reshape(ends, steps, cases)

    taps_t = jnp.transpose(impulse_taps[:steps])
    base_t = jnp.transpose(base[steps:])
    hist_list = []
    for t in range(steps, total):
        history = base_t[:, t - steps][:, None]
        for j in range(t - steps + 1):
            history = history + taps_t[:, j][:, None] * far[:, t - steps - j]
        hist_list.append(history)
    hist1 = jnp.stack(hist_list, axis=1).reshape(ends, steps * cases)
    node_hist = mm("nk,km->nm", attach_mapT, hist1).reshape(subnets, rows, steps, cases)
    angle1 = jnp.asarray(omega_step * np.arange(steps, total), jnp.float32)
    phase = jnp.cos(angle1[None, None, :] + source_angle[:, :, None])
    inj1 = amp_t[:, :, None, :] * phase[:, :, :, None] + node_hist
    part1 = jnp.sum(fault_col[:, :, None, :] * inj1, axis=1)
    part1 = lax.all_to_all(jnp.broadcast_to(part1[None], (n_node,) + part1.shape), "node", 0, 0, tiled=True)
    sums1 = jnp.sum(part1, axis=0)
    gathered1 = lax.all_gather(inj1.reshape(subnets, rows, steps * cases), "node", axis=1, tiled=True)
    prod1 = fast("srj,sjm->srm", impedance, gathered1).reshape(subnets, rows, steps, cases)
    t1 = t0 + steps
    current1 = jnp.where(fault_step[:, None, :] <= t1[None, :, None], sums1 / denominator[:, None, :], 0.0)
    volt1 = prod1 - current1[:, None] * fault_col[:, :, None, :]
    volt = jnp.concatenate([volt0, volt1], axis=2)
    return jnp.transpose(volt, (2, 0, 3, 1))


def solution(mesh):
    in_specs = (
        P("region", "node", None),
        P("region", None, "node"),
        P("region", "node"),
        P(None, ("region", "node")),
        P(None, ("region", "node")),
        P(("region", "node")),
        P(("region", "node")),
        P(("region", "node"), None),
        P("region", None),
        P("region", None),
        P("region", None),
    )
    out_specs = P(None, "region", None, "node")
    return jax.shard_map(body, mesh=mesh, in_specs=in_specs, out_specs=out_specs, check_vma=False)
```

```python
import math

import jax
import numpy as np
import jax.numpy as jnp
from jax import lax
from jax.sharding import PartitionSpec as P

WINDOW_STEPS = 4
WINDOW_COUNT = 2


omega_step = 2.0 * math.pi / 400.0
PRECISE = lax.Precision.HIGHEST


def mm(spec, a, b):
    return jnp.einsum(spec, a, b, precision=PRECISE, preferred_element_type=jnp.float32)


def fast(spec, a, b):
    return jnp.einsum(spec, a, b, precision=lax.Precision.HIGH, preferred_element_type=jnp.float32)


def body(
    impedance,
    source_amp,
    source_angle,
    impulse_taps,
    incident,
    conductance,
    attach,
    pair_slot,
    fault_node,
    fault_step,
    fault_res,
):
    subnets, rows, order = impedance.shape
    cases = source_amp.shape[1]
    tap_len, ends = impulse_taps.shape
    past = incident.shape[0]
    steps = WINDOW_STEPS
    total = WINDOW_STEPS * WINDOW_COUNT
    n_node = order // rows
    local = subnets * rows
    row_ids = lax.axis_index("node") * rows + lax.iota(jnp.int32, rows)

    amp_t = jnp.transpose(source_amp, (0, 2, 1))
    amp_full = lax.all_gather(lax.optimization_barrier(source_amp), "node", axis=2, tiled=True)
    amp_cos = amp_t * jnp.cos(source_angle)[:, :, None]
    amp_sin = amp_t * jnp.sin(source_angle)[:, :, None]

    local_ids = lax.iota(jnp.int32, local)
    attach_map = (attach[:, None] == local_ids[None, :]).astype(jnp.float32)
    attach_mapT = (local_ids[:, None] == attach[None, :]).astype(jnp.float32)

    onehotT = (lax.iota(jnp.int32, order)[None, :, None] == fault_node[:, None, :]).astype(jnp.float32)
    fault_col = mm("srj,sjc->src", impedance, onehotT)
    owner = (row_ids[None, :, None] == fault_node[:, None, :]).astype(jnp.float32)
    self_part = jnp.sum(fault_col * owner, axis=1)

    flip = (lax.iota(jnp.int32, tap_len)[:, None] + lax.iota(jnp.int32, tap_len)[None, :] == tap_len - 1).astype(
        jnp.float32
    )
    taps_rev = mm("uj,jk->uk", flip, impulse_taps)
    padded = jnp.concatenate([incident, jnp.zeros((tap_len + total - 1 - past, ends), jnp.float32)], axis=0)
    base = jnp.stack([jnp.sum(taps_rev * padded[t : t + tap_len], axis=0) for t in range(total)])
    base_node = mm("tk,kn->tn", base[:steps], attach_map).reshape(steps, subnets, rows)
    h0 = jnp.transpose(base_node, (1, 0, 2))

    part_cos = jnp.sum(fault_col * amp_cos, axis=1)
    part_sin = jnp.sum(fault_col * amp_sin, axis=1)
    part_h = mm("sic,sti->stc", fault_col, h0)
    partials = jnp.concatenate(
        [part_cos[:, None], part_sin[:, None], part_h, self_part[:, None]], axis=1
    ).reshape(subnets, -1)
    pad_len = 2 * rows - partials.shape[1]
    partials = jnp.concatenate([partials, jnp.zeros((subnets, pad_len), jnp.float32)], axis=1)
    small = jnp.concatenate(
        [h0, partials.reshape(subnets, 2, rows), source_angle[:, None], jnp.zeros((subnets, 1, rows), jnp.float32)],
        axis=1,
    )
    small = jnp.broadcast_to(small[None], (n_node,) + small.shape)
    small = lax.all_to_all(small, "node", 0, 0, tiled=True)
    h0_full = jnp.transpose(small[:, :, :steps], (1, 0, 3, 2)).reshape(subnets, order, steps)
    sums = jnp.sum(small[:, :, steps : steps + 2], axis=0).reshape(subnets, 2 * rows)
    angle_full = jnp.transpose(small[:, :, steps + 2], (1, 0, 2)).reshape(subnets, order)
    sources = jnp.concatenate(
        [amp_full * jnp.cos(angle_full)[:, None, :], amp_full * jnp.sin(angle_full)[:, None, :]], axis=1
    )
    sums = sums[:, : 7 * cases].reshape(subnets, 7, cases)
    denominator = sums[:, 6] + fault_res

    prod = fast("srj,scj->src", impedance, sources)
    prod_h = fast("srj,sjt->srt", impedance, h0_full)
    t0 = lax.iota(jnp.int32, steps)
    cw = jnp.asarray(np.cos(omega_step * np.arange(steps)), jnp.float32)
    sw = jnp.asarray(np.sin(omega_step * np.arange(steps)), jnp.float32)
    open0 = (
        cw[None, None, :, None] * prod[:, :, None, :cases]
        - sw[None, None, :, None] * prod[:, :, None, cases:]
        + prod_h[:, :, :, None]
    )
    fault0 = cw[None, :, None] * sums[:, 0][:, None] - sw[None, :, None] * sums[:, 1][:, None] + sums[:, 2 : 2 + steps]
    current0 = jnp.where(fault_step[:, None, :] <= t0[None, :, None], fault0 / denominator[:, None, :], 0.0)
    volt0 = open0 - current0[:, None] * fault_col[:, :, None, :]

    at_ends = mm("kn,nm->km", attach_map, volt0.reshape(local, steps * cases)).reshape(ends, steps, cases)
    waves = 2.0 * conductance[:, None, None] * at_ends - jnp.transpose(base[:steps])[:, :, None]

    slot_row = pair_slot[0]
    end_ids = lax.iota(jnp.int32, ends)
    selector = (end_ids[:, None] == slot_row[None, :]).astype(jnp.float32)
    selectorT = (slot_row[:, None] == end_ids[None, :]).astype(jnp.float32)
    outgoing = mm("pk,km->pm", selectorT, waves.reshape(ends, steps * cases))
    incoming = lax.all_to_all(outgoing, ("region", "node"), 0, 0, tiled=True)
    far = mm("kp,pm->km", selector, incoming).reshape(ends, steps, cases)

    taps_t = jnp.transpose(impulse_taps[:steps])
    base_t = jnp.transpose(base[steps:])
    hist_list = []
    for t in range(steps, total):
        history = base_t[:, t - steps][:, None]
        for j in range(t - steps + 1):
            history = history + taps_t[:, j][:, None] * far[:, t - steps - j]
        hist_list.append(history)
    hist1 = jnp.stack(hist_list, axis=1).reshape(ends, steps * cases)
    node_hist = mm("nk,km->nm", attach_mapT, hist1).reshape(subnets, rows, steps, cases)
    angle1 = jnp.asarray(omega_step * np.arange(steps, total), jnp.float32)
    phase = jnp.cos(angle1[None, None, :] + source_angle[:, :, None])
    inj1 = amp_t[:, :, None, :] * phase[:, :, :, None] + node_hist
    part1 = jnp.sum(fault_col[:, :, None, :] * inj1, axis=1)
    part1 = lax.all_to_all(jnp.broadcast_to(part1[None], (n_node,) + part1.shape), "node", 0, 0, tiled=True)
    sums1 = jnp.sum(part1, axis=0)
    gathered1 = lax.all_gather(inj1.reshape(subnets, rows, steps * cases), "node", axis=1, tiled=True)
    prod1 = fast("srj,sjm->srm", impedance, gathered1).reshape(subnets, rows, steps, cases)
    t1 = t0 + steps
    current1 = jnp.where(fault_step[:, None, :] <= t1[None, :, None], sums1 / denominator[:, None, :], 0.0)
    volt1 = prod1 - current1[:, None] * fault_col[:, :, None, :]
    volt = jnp.concatenate([volt0, volt1], axis=2)
    return jnp.transpose(volt, (2, 0, 3, 1))


def solution(mesh):
    in_specs = (
        P("region", "node", None),
        P("region", None, "node"),
        P("region", "node"),
        P(None, ("region", "node")),
        P(None, ("region", "node")),
        P(("region", "node")),
        P(("region", "node")),
        P(("region", "node"), None),
        P("region", None),
        P("region", None),
        P("region", None),
    )
    out_specs = P(None, "region", None, "node")
    return jax.shard_map(body, mesh=mesh, in_specs=in_specs, out_specs=out_specs, check_vma=False)
```

```python
import math

import jax
import numpy as np
import jax.numpy as jnp
from jax import lax
from jax.sharding import PartitionSpec as P

WINDOW_STEPS = 4
WINDOW_COUNT = 2


omega_step = 2.0 * math.pi / 400.0
PRECISE = lax.Precision.HIGHEST


def mm(spec, a, b):
    return jnp.einsum(spec, a, b, precision=PRECISE, preferred_element_type=jnp.float32)


def pick(spec, a, b):
    return jnp.einsum(spec, a, b, precision=lax.Precision.HIGH, preferred_element_type=jnp.float32)


def fast(spec, a, b):
    return jnp.einsum(spec, a, b, precision=lax.Precision.HIGH, preferred_element_type=jnp.float32)


def body(
    impedance,
    source_amp,
    source_angle,
    impulse_taps,
    incident,
    conductance,
    attach,
    pair_slot,
    fault_node,
    fault_step,
    fault_res,
):
    subnets, rows, order = impedance.shape
    cases = source_amp.shape[1]
    tap_len, ends = impulse_taps.shape
    past = incident.shape[0]
    steps = WINDOW_STEPS
    total = WINDOW_STEPS * WINDOW_COUNT
    n_node = order // rows
    local = subnets * rows
    row_ids = lax.axis_index("node") * rows + lax.iota(jnp.int32, rows)

    amp_t = jnp.transpose(source_amp, (0, 2, 1))
    amp_full = lax.all_gather(lax.optimization_barrier(source_amp), "node", axis=2, tiled=True)
    amp_cos = amp_t * jnp.cos(source_angle)[:, :, None]
    amp_sin = amp_t * jnp.sin(source_angle)[:, :, None]

    local_ids = lax.iota(jnp.int32, local)
    attach_map = (attach[:, None] == local_ids[None, :]).astype(jnp.float32)
    attach_mapT = (local_ids[:, None] == attach[None, :]).astype(jnp.float32)

    onehotT = (lax.iota(jnp.int32, order)[None, :, None] == fault_node[:, None, :]).astype(jnp.float32)
    fault_col = mm("srj,sjc->src", impedance, onehotT)
    owner = (row_ids[None, :, None] == fault_node[:, None, :]).astype(jnp.float32)
    self_part = jnp.sum(fault_col * owner, axis=1)

    flip = (lax.iota(jnp.int32, tap_len)[:, None] + lax.iota(jnp.int32, tap_len)[None, :] == tap_len - 1).astype(
        jnp.float32
    )
    taps_rev = mm("uj,jk->uk", flip, impulse_taps)
    padded = jnp.concatenate([incident, jnp.zeros((tap_len + total - 1 - past, ends), jnp.float32)], axis=0)
    base = jnp.stack([jnp.sum(taps_rev * padded[t : t + tap_len], axis=0) for t in range(total)])
    base_node = mm("tk,kn->tn", base[:steps], attach_map).reshape(steps, subnets, rows)
    h0 = jnp.transpose(base_node, (1, 0, 2))

    part_cos = jnp.sum(fault_col * amp_cos, axis=1)
    part_sin = jnp.sum(fault_col * amp_sin, axis=1)
    part_h = mm("sic,sti->stc", fault_col, h0)
    partials = jnp.concatenate(
        [part_cos[:, None], part_sin[:, None], part_h, self_part[:, None]], axis=1
    ).reshape(subnets, -1)
    pad_len = 2 * rows - partials.shape[1]
    partials = jnp.concatenate([partials, jnp.zeros((subnets, pad_len), jnp.float32)], axis=1)
    small = jnp.concatenate(
        [h0, partials.reshape(subnets, 2, rows), source_angle[:, None], jnp.zeros((subnets, 1, rows), jnp.float32)],
        axis=1,
    )
    small = jnp.broadcast_to(small[None], (n_node,) + small.shape)
    small = lax.all_to_all(small, "node", 0, 0, tiled=True)
    h0_full = jnp.transpose(small[:, :, :steps], (1, 0, 3, 2)).reshape(subnets, order, steps)
    sums = jnp.sum(small[:, :, steps : steps + 2], axis=0).reshape(subnets, 2 * rows)
    angle_full = jnp.transpose(small[:, :, steps + 2], (1, 0, 2)).reshape(subnets, order)
    sources = jnp.concatenate(
        [amp_full * jnp.cos(angle_full)[:, None, :], amp_full * jnp.sin(angle_full)[:, None, :]], axis=1
    )
    sums = sums[:, : 7 * cases].reshape(subnets, 7, cases)
    denominator = sums[:, 6] + fault_res

    prod = fast("srj,scj->src", impedance, sources)
    prod_h = fast("srj,sjt->srt", impedance, h0_full)
    t0 = lax.iota(jnp.int32, steps)
    cw = jnp.asarray(np.cos(omega_step * np.arange(steps)), jnp.float32)
    sw = jnp.asarray(np.sin(omega_step * np.arange(steps)), jnp.float32)
    open0 = (
        cw[None, None, :, None] * prod[:, :, None, :cases]
        - sw[None, None, :, None] * prod[:, :, None, cases:]
        + prod_h[:, :, :, None]
    )
    fault0 = cw[None, :, None] * sums[:, 0][:, None] - sw[None, :, None] * sums[:, 1][:, None] + sums[:, 2 : 2 + steps]
    current0 = jnp.where(fault_step[:, None, :] <= t0[None, :, None], fault0 / denominator[:, None, :], 0.0)
    volt0 = open0 - current0[:, None] * fault_col[:, :, None, :]

    at_ends = pick("kn,nm->km", attach_map, volt0.reshape(local, steps * cases)).reshape(ends, steps, cases)
    waves = 2.0 * conductance[:, None, None] * at_ends - jnp.transpose(base[:steps])[:, :, None]

    slot_row = pair_slot[0]
    end_ids = lax.iota(jnp.int32, ends)
    selector = (end_ids[:, None] == slot_row[None, :]).astype(jnp.float32)
    selectorT = (slot_row[:, None] == end_ids[None, :]).astype(jnp.float32)
    outgoing = pick("pk,km->pm", selectorT, waves.reshape(ends, steps * cases))
    incoming = lax.all_to_all(outgoing, ("region", "node"), 0, 0, tiled=True)
    far = pick("kp,pm->km", selector, incoming).reshape(ends, steps, cases)

    taps_t = jnp.transpose(impulse_taps[:steps])
    base_t = jnp.transpose(base[steps:])
    hist_list = []
    for t in range(steps, total):
        history = base_t[:, t - steps][:, None]
        for j in range(t - steps + 1):
            history = history + taps_t[:, j][:, None] * far[:, t - steps - j]
        hist_list.append(history)
    hist1 = jnp.stack(hist_list, axis=1).reshape(ends, steps * cases)
    node_hist = pick("nk,km->nm", attach_mapT, hist1).reshape(subnets, rows, steps, cases)
    angle1 = jnp.asarray(omega_step * np.arange(steps, total), jnp.float32)
    phase = jnp.cos(angle1[None, None, :] + source_angle[:, :, None])
    inj1 = amp_t[:, :, None, :] * phase[:, :, :, None] + node_hist
    part1 = jnp.sum(fault_col[:, :, None, :] * inj1, axis=1)
    part1 = lax.all_to_all(jnp.broadcast_to(part1[None], (n_node,) + part1.shape), "node", 0, 0, tiled=True)
    sums1 = jnp.sum(part1, axis=0)
    gathered1 = lax.all_gather(inj1.reshape(subnets, rows, steps * cases), "node", axis=1, tiled=True)
    prod1 = fast("srj,sjm->srm", impedance, gathered1).reshape(subnets, rows, steps, cases)
    t1 = t0 + steps
    current1 = jnp.where(fault_step[:, None, :] <= t1[None, :, None], sums1 / denominator[:, None, :], 0.0)
    volt1 = prod1 - current1[:, None] * fault_col[:, :, None, :]
    volt = jnp.concatenate([volt0, volt1], axis=2)
    return jnp.transpose(volt, (2, 0, 3, 1))


def solution(mesh):
    in_specs = (
        P("region", "node", None),
        P("region", None, "node"),
        P("region", "node"),
        P(None, ("region", "node")),
        P(None, ("region", "node")),
        P(("region", "node")),
        P(("region", "node")),
        P(("region", "node"), None),
        P("region", None),
        P("region", None),
        P("region", None),
    )
    out_specs = P(None, "region", None, "node")
    return jax.shard_map(body, mesh=mesh, in_specs=in_specs, out_specs=out_specs, check_vma=False)
```

```python
import math

import jax
import numpy as np
import jax.numpy as jnp
from jax import lax
from jax.sharding import PartitionSpec as P

WINDOW_STEPS = 4
WINDOW_COUNT = 2


omega_step = 2.0 * math.pi / 400.0
PRECISE = lax.Precision.HIGHEST


def mm(spec, a, b):
    return jnp.einsum(spec, a, b, precision=PRECISE, preferred_element_type=jnp.float32)


def pick(spec, a, b):
    return jnp.einsum(spec, a, b, precision=lax.Precision.HIGH, preferred_element_type=jnp.float32)


def fast(spec, a, b):
    return jnp.einsum(spec, a, b, precision=lax.Precision.HIGH, preferred_element_type=jnp.float32)


def body(
    impedance,
    source_amp,
    source_angle,
    impulse_taps,
    incident,
    conductance,
    attach,
    pair_slot,
    fault_node,
    fault_step,
    fault_res,
):
    subnets, rows, order = impedance.shape
    cases = source_amp.shape[1]
    tap_len, ends = impulse_taps.shape
    past = incident.shape[0]
    steps = WINDOW_STEPS
    total = WINDOW_STEPS * WINDOW_COUNT
    n_node = order // rows
    local = subnets * rows
    row_ids = lax.axis_index("node") * rows + lax.iota(jnp.int32, rows)

    amp_t = jnp.transpose(source_amp, (0, 2, 1))
    amp_full = lax.all_gather(lax.optimization_barrier(source_amp), "node", axis=2, tiled=True)
    amp_cos = amp_t * jnp.cos(source_angle)[:, :, None]
    amp_sin = amp_t * jnp.sin(source_angle)[:, :, None]

    local_ids = lax.iota(jnp.int32, local)
    attach_map = (attach[:, None] == local_ids[None, :]).astype(jnp.float32)
    attach_mapT = (local_ids[:, None] == attach[None, :]).astype(jnp.float32)

    onehotT = (lax.iota(jnp.int32, order)[None, :, None] == fault_node[:, None, :]).astype(jnp.float32)
    fault_col = mm("srj,sjc->src", impedance, onehotT)
    owner = (row_ids[None, :, None] == fault_node[:, None, :]).astype(jnp.float32)
    self_part = jnp.sum(fault_col * owner, axis=1)

    flip = (lax.iota(jnp.int32, tap_len)[:, None] + lax.iota(jnp.int32, tap_len)[None, :] == tap_len - 1).astype(
        jnp.float32
    )
    taps_rev = mm("uj,jk->uk", flip, impulse_taps)
    padded = jnp.concatenate([incident, jnp.zeros((tap_len + total - 1 - past, ends), jnp.float32)], axis=0)
    base = jnp.stack([jnp.sum(taps_rev * padded[t : t + tap_len], axis=0) for t in range(total)])
    base_node = mm("tk,kn->tn", base[:steps], attach_map).reshape(steps, subnets, rows)
    h0 = jnp.transpose(base_node, (1, 0, 2))

    part_cos = jnp.sum(fault_col * amp_cos, axis=1)
    part_sin = jnp.sum(fault_col * amp_sin, axis=1)
    part_h = mm("sic,sti->stc", fault_col, h0)
    partials = jnp.concatenate(
        [part_cos[:, None], part_sin[:, None], part_h, self_part[:, None]], axis=1
    ).reshape(subnets, -1)
    pad_len = 2 * rows - partials.shape[1]
    partials = jnp.concatenate([partials, jnp.zeros((subnets, pad_len), jnp.float32)], axis=1)
    small = jnp.concatenate(
        [h0, partials.reshape(subnets, 2, rows), source_angle[:, None], jnp.zeros((subnets, 1, rows), jnp.float32)],
        axis=1,
    )
    small = jnp.broadcast_to(small[None], (n_node,) + small.shape)
    small = lax.all_to_all(small, "node", 0, 0, tiled=True)
    h0_full = jnp.transpose(small[:, :, :steps], (1, 0, 3, 2)).reshape(subnets, order, steps)
    sums = jnp.sum(small[:, :, steps : steps + 2], axis=0).reshape(subnets, 2 * rows)
    angle_full = jnp.transpose(small[:, :, steps + 2], (1, 0, 2)).reshape(subnets, order)
    sources = jnp.concatenate(
        [amp_full * jnp.cos(angle_full)[:, None, :], amp_full * jnp.sin(angle_full)[:, None, :]], axis=1
    )
    sums = sums[:, : 7 * cases].reshape(subnets, 7, cases)
    denominator = sums[:, 6] + fault_res

    prod = fast("srj,scj->src", impedance, sources)
    prod_h = fast("srj,sjt->srt", impedance, h0_full)
    t0 = lax.iota(jnp.int32, steps)
    cw = jnp.asarray(np.cos(omega_step * np.arange(steps)), jnp.float32)
    sw = jnp.asarray(np.sin(omega_step * np.arange(steps)), jnp.float32)
    open0 = (
        cw[None, None, :, None] * prod[:, :, None, :cases]
        - sw[None, None, :, None] * prod[:, :, None, cases:]
        + prod_h[:, :, :, None]
    )
    fault0 = cw[None, :, None] * sums[:, 0][:, None] - sw[None, :, None] * sums[:, 1][:, None] + sums[:, 2 : 2 + steps]
    current0 = jnp.where(fault_step[:, None, :] <= t0[None, :, None], fault0 / denominator[:, None, :], 0.0)
    volt0 = open0 - current0[:, None] * fault_col[:, :, None, :]

    at_ends = pick("kn,nm->km", attach_map, volt0.reshape(local, steps * cases)).reshape(ends, steps, cases)
    waves = 2.0 * conductance[:, None, None] * at_ends - jnp.transpose(base[:steps])[:, :, None]

    slot_row = pair_slot[0]
    end_ids = lax.iota(jnp.int32, ends)
    selector = (end_ids[:, None] == slot_row[None, :]).astype(jnp.float32)
    selectorT = (slot_row[:, None] == end_ids[None, :]).astype(jnp.float32)
    outgoing = pick("pk,km->mp", selectorT, waves.reshape(ends, steps * cases))
    incoming = lax.all_to_all(outgoing, ("region", "node"), 1, 1, tiled=True)
    far = pick("kp,mp->km", selector, incoming).reshape(ends, steps, cases)

    taps_t = jnp.transpose(impulse_taps[:steps])
    base_t = jnp.transpose(base[steps:])
    hist_list = []
    for t in range(steps, total):
        history = base_t[:, t - steps][:, None]
        for j in range(t - steps + 1):
            history = history + taps_t[:, j][:, None] * far[:, t - steps - j]
        hist_list.append(history)
    hist1 = jnp.stack(hist_list, axis=1).reshape(ends, steps * cases)
    node_hist = pick("nk,km->nm", attach_mapT, hist1).reshape(subnets, rows, steps, cases)
    angle1 = jnp.asarray(omega_step * np.arange(steps, total), jnp.float32)
    phase = jnp.cos(angle1[None, None, :] + source_angle[:, :, None])
    inj1 = amp_t[:, :, None, :] * phase[:, :, :, None] + node_hist
    part1 = jnp.sum(fault_col[:, :, None, :] * inj1, axis=1)
    part1 = lax.all_to_all(jnp.broadcast_to(part1[None], (n_node,) + part1.shape), "node", 0, 0, tiled=True)
    sums1 = jnp.sum(part1, axis=0)
    gathered1 = lax.all_gather(inj1.reshape(subnets, rows, steps * cases), "node", axis=1, tiled=True)
    prod1 = fast("srj,sjm->srm", impedance, gathered1).reshape(subnets, rows, steps, cases)
    t1 = t0 + steps
    current1 = jnp.where(fault_step[:, None, :] <= t1[None, :, None], sums1 / denominator[:, None, :], 0.0)
    volt1 = prod1 - current1[:, None] * fault_col[:, :, None, :]
    volt = jnp.concatenate([volt0, volt1], axis=2)
    return jnp.transpose(volt, (2, 0, 3, 1))


def solution(mesh):
    in_specs = (
        P("region", "node", None),
        P("region", None, "node"),
        P("region", "node"),
        P(None, ("region", "node")),
        P(None, ("region", "node")),
        P(("region", "node")),
        P(("region", "node")),
        P(("region", "node"), None),
        P("region", None),
        P("region", None),
        P("region", None),
    )
    out_specs = P(None, "region", None, "node")
    return jax.shard_map(body, mesh=mesh, in_specs=in_specs, out_specs=out_specs, check_vma=False)
```

```python
import math

import jax
import numpy as np
import jax.numpy as jnp
from jax import lax
from jax.sharding import PartitionSpec as P

WINDOW_STEPS = 4
WINDOW_COUNT = 2


omega_step = 2.0 * math.pi / 400.0
PRECISE = lax.Precision.HIGHEST


def mm(spec, a, b):
    return jnp.einsum(spec, a, b, precision=PRECISE, preferred_element_type=jnp.float32)


def pick(spec, a, b):
    return jnp.einsum(spec, a, b, precision=lax.Precision.HIGH, preferred_element_type=jnp.float32)


def fast(spec, a, b):
    return jnp.einsum(spec, a, b, precision=lax.Precision.HIGH, preferred_element_type=jnp.float32)


def body(
    impedance,
    source_amp,
    source_angle,
    impulse_taps,
    incident,
    conductance,
    attach,
    pair_slot,
    fault_node,
    fault_step,
    fault_res,
):
    subnets, rows, order = impedance.shape
    cases = source_amp.shape[1]
    tap_len, ends = impulse_taps.shape
    past = incident.shape[0]
    steps = WINDOW_STEPS
    total = WINDOW_STEPS * WINDOW_COUNT
    n_node = order // rows
    local = subnets * rows
    row_ids = lax.axis_index("node") * rows + lax.iota(jnp.int32, rows)

    amp_t = jnp.transpose(source_amp, (0, 2, 1))
    amp_full = lax.all_gather(lax.optimization_barrier(source_amp), "node", axis=2, tiled=True)
    amp_cos = amp_t * jnp.cos(source_angle)[:, :, None]
    amp_sin = amp_t * jnp.sin(source_angle)[:, :, None]

    local_ids = lax.iota(jnp.int32, local)
    attach_map = (attach[:, None] == local_ids[None, :]).astype(jnp.float32)
    attach_mapT = (local_ids[:, None] == attach[None, :]).astype(jnp.float32)

    onehotT = (lax.iota(jnp.int32, order)[None, :, None] == fault_node[:, None, :]).astype(jnp.float32)
    fault_col = mm("srj,sjc->src", impedance, onehotT)
    owner = (row_ids[None, :, None] == fault_node[:, None, :]).astype(jnp.float32)
    self_part = jnp.sum(fault_col * owner, axis=1)

    flip = (lax.iota(jnp.int32, tap_len)[:, None] + lax.iota(jnp.int32, tap_len)[None, :] == tap_len - 1).astype(
        jnp.float32
    )
    taps_rev = mm("uj,jk->uk", flip, impulse_taps)
    padded = jnp.concatenate([incident, jnp.zeros((tap_len + total - 1 - past, ends), jnp.float32)], axis=0)
    base = jnp.stack([jnp.sum(taps_rev * padded[t : t + tap_len], axis=0) for t in range(total)])
    base_node = mm("tk,kn->tn", base[:steps], attach_map).reshape(steps, subnets, rows)
    h0 = jnp.transpose(base_node, (1, 0, 2))

    part_cos = jnp.sum(fault_col * amp_cos, axis=1)
    part_sin = jnp.sum(fault_col * amp_sin, axis=1)
    part_h = mm("sic,sti->stc", fault_col, h0)
    partials = jnp.concatenate(
        [part_cos[:, None], part_sin[:, None], part_h, self_part[:, None]], axis=1
    ).reshape(subnets, -1)
    pad_len = 2 * rows - partials.shape[1]
    partials = jnp.concatenate([partials, jnp.zeros((subnets, pad_len), jnp.float32)], axis=1)
    small = jnp.concatenate(
        [h0, partials.reshape(subnets, 2, rows), source_angle[:, None], jnp.zeros((subnets, 1, rows), jnp.float32)],
        axis=1,
    )
    small = jnp.broadcast_to(small[None], (n_node,) + small.shape)
    small = lax.all_to_all(small, "node", 0, 0, tiled=True)
    h0_full = jnp.transpose(small[:, :, :steps], (1, 0, 3, 2)).reshape(subnets, order, steps)
    sums = jnp.sum(small[:, :, steps : steps + 2], axis=0).reshape(subnets, 2 * rows)
    angle_full = jnp.transpose(small[:, :, steps + 2], (1, 0, 2)).reshape(subnets, order)
    sources = jnp.concatenate(
        [amp_full * jnp.cos(angle_full)[:, None, :], amp_full * jnp.sin(angle_full)[:, None, :]], axis=1
    )
    sums = sums[:, : 7 * cases].reshape(subnets, 7, cases)
    denominator = sums[:, 6] + fault_res

    prod = fast("srj,scj->src", impedance, sources)
    prod_h = fast("srj,sjt->srt", impedance, h0_full)
    t0 = lax.iota(jnp.int32, steps)
    cw = jnp.asarray(np.cos(omega_step * np.arange(steps)), jnp.float32)
    sw = jnp.asarray(np.sin(omega_step * np.arange(steps)), jnp.float32)
    open0 = (
        cw[None, None, :, None] * prod[:, :, None, :cases]
        - sw[None, None, :, None] * prod[:, :, None, cases:]
        + prod_h[:, :, :, None]
    )
    fault0 = cw[None, :, None] * sums[:, 0][:, None] - sw[None, :, None] * sums[:, 1][:, None] + sums[:, 2 : 2 + steps]
    current0 = jnp.where(fault_step[:, None, :] <= t0[None, :, None], fault0 / denominator[:, None, :], 0.0)
    volt0 = open0 - current0[:, None] * fault_col[:, :, None, :]

    at_ends = pick("kn,nm->km", attach_map, volt0.reshape(local, steps * cases)).reshape(ends, steps, cases)
    waves = 2.0 * conductance[:, None, None] * at_ends - jnp.transpose(base[:steps])[:, :, None]

    slot_row = pair_slot[0]
    end_ids = lax.iota(jnp.int32, ends)
    selector = (end_ids[:, None] == slot_row[None, :]).astype(jnp.float32)
    selectorT = (slot_row[:, None] == end_ids[None, :]).astype(jnp.float32)
    outgoing = pick("pk,km->pm", selectorT, waves.reshape(ends, steps * cases))
    incoming = lax.all_to_all(outgoing, ("region", "node"), 0, 0, tiled=True)
    far = pick("kp,pm->km", selector, incoming).reshape(ends, steps, cases)

    taps_t = jnp.transpose(impulse_taps[:steps])
    base_t = jnp.transpose(base[steps:])
    hist_list = []
    for t in range(steps, total):
        history = base_t[:, t - steps][:, None]
        for j in range(t - steps + 1):
            history = history + taps_t[:, j][:, None] * far[:, t - steps - j]
        hist_list.append(history)
    hist1 = jnp.stack(hist_list, axis=1).reshape(ends, steps * cases)
    node_hist = pick("nk,km->nm", attach_mapT, hist1).reshape(subnets, rows, steps, cases)
    angle1 = jnp.asarray(omega_step * np.arange(steps, total), jnp.float32)
    phase = jnp.cos(angle1[None, None, :] + source_angle[:, :, None])
    inj1 = amp_t[:, :, None, :] * phase[:, :, :, None] + node_hist
    part1 = jnp.sum(fault_col[:, :, None, :] * inj1, axis=1)
    part1 = lax.all_to_all(jnp.broadcast_to(part1[None], (n_node,) + part1.shape), "node", 0, 0, tiled=True)
    sums1 = jnp.sum(part1, axis=0)
    gathered1 = lax.all_gather(inj1.reshape(subnets, rows, steps * cases), "node", axis=1, tiled=True)
    prod1 = fast("srj,sjm->smr", impedance, gathered1).reshape(subnets, steps, cases, rows)
    t1 = t0 + steps
    current1 = jnp.where(fault_step[:, None, :] <= t1[None, :, None], sums1 / denominator[:, None, :], 0.0)
    volt1 = prod1 - current1[..., None] * jnp.transpose(fault_col, (0, 2, 1))[:, None]
    return jnp.concatenate([jnp.transpose(volt0, (2, 0, 3, 1)), jnp.transpose(volt1, (1, 0, 2, 3))], axis=0)


def solution(mesh):
    in_specs = (
        P("region", "node", None),
        P("region", None, "node"),
        P("region", "node"),
        P(None, ("region", "node")),
        P(None, ("region", "node")),
        P(("region", "node")),
        P(("region", "node")),
        P(("region", "node"), None),
        P("region", None),
        P("region", None),
        P("region", None),
    )
    out_specs = P(None, "region", None, "node")
    return jax.shard_map(body, mesh=mesh, in_specs=in_specs, out_specs=out_specs, check_vma=False)
```

```python
import math

import jax
import numpy as np
import jax.numpy as jnp
from jax import lax
from jax.sharding import PartitionSpec as P

WINDOW_STEPS = 4
WINDOW_COUNT = 2


omega_step = 2.0 * math.pi / 400.0
PRECISE = lax.Precision.HIGHEST


def mm(spec, a, b):
    return jnp.einsum(spec, a, b, precision=PRECISE, preferred_element_type=jnp.float32)


def pick(spec, a, b):
    return jnp.einsum(spec, a, b, precision=lax.Precision.HIGH, preferred_element_type=jnp.float32)


def fast(spec, a, b):
    return jnp.einsum(spec, a, b, precision=lax.Precision.HIGH, preferred_element_type=jnp.float32)


def body(
    impedance,
    source_amp,
    source_angle,
    impulse_taps,
    incident,
    conductance,
    attach,
    pair_slot,
    fault_node,
    fault_step,
    fault_res,
):
    subnets, rows, order = impedance.shape
    cases = source_amp.shape[1]
    tap_len, ends = impulse_taps.shape
    past = incident.shape[0]
    steps = WINDOW_STEPS
    total = WINDOW_STEPS * WINDOW_COUNT
    n_node = order // rows
    local = subnets * rows
    row_ids = lax.axis_index("node") * rows + lax.iota(jnp.int32, rows)

    amp_t = jnp.transpose(source_amp, (0, 2, 1))
    amp_full = lax.all_gather(lax.optimization_barrier(source_amp), "node", axis=2, tiled=True)
    amp_cos = amp_t * jnp.cos(source_angle)[:, :, None]
    amp_sin = amp_t * jnp.sin(source_angle)[:, :, None]

    local_ids = lax.iota(jnp.int32, local)
    attach_map = (attach[:, None] == local_ids[None, :]).astype(jnp.float32)
    attach_mapT = (local_ids[:, None] == attach[None, :]).astype(jnp.float32)

    onehotT = (lax.iota(jnp.int32, order)[None, :, None] == fault_node[:, None, :]).astype(jnp.float32)
    fault_col = pick("srj,sjc->src", impedance, onehotT)
    owner = (row_ids[None, :, None] == fault_node[:, None, :]).astype(jnp.float32)
    self_part = jnp.sum(fault_col * owner, axis=1)

    flip = (lax.iota(jnp.int32, tap_len)[:, None] + lax.iota(jnp.int32, tap_len)[None, :] == tap_len - 1).astype(
        jnp.float32
    )
    taps_rev = mm("uj,jk->uk", flip, impulse_taps)
    padded = jnp.concatenate([incident, jnp.zeros((tap_len + total - 1 - past, ends), jnp.float32)], axis=0)
    base = jnp.stack([jnp.sum(taps_rev * padded[t : t + tap_len], axis=0) for t in range(total)])
    base_node = mm("tk,kn->tn", base[:steps], attach_map).reshape(steps, subnets, rows)
    h0 = jnp.transpose(base_node, (1, 0, 2))

    part_cos = jnp.sum(fault_col * amp_cos, axis=1)
    part_sin = jnp.sum(fault_col * amp_sin, axis=1)
    part_h = mm("sic,sti->stc", fault_col, h0)
    partials = jnp.concatenate(
        [part_cos[:, None], part_sin[:, None], part_h, self_part[:, None]], axis=1
    ).reshape(subnets, -1)
    pad_len = 2 * rows - partials.shape[1]
    partials = jnp.concatenate([partials, jnp.zeros((subnets, pad_len), jnp.float32)], axis=1)
    small = jnp.concatenate(
        [h0, partials.reshape(subnets, 2, rows), source_angle[:, None], jnp.zeros((subnets, 1, rows), jnp.float32)],
        axis=1,
    )
    small = jnp.broadcast_to(small[None], (n_node,) + small.shape)
    small = lax.all_to_all(small, "node", 0, 0, tiled=True)
    h0_full = jnp.transpose(small[:, :, :steps], (1, 0, 3, 2)).reshape(subnets, order, steps)
    sums = jnp.sum(small[:, :, steps : steps + 2], axis=0).reshape(subnets, 2 * rows)
    angle_full = jnp.transpose(small[:, :, steps + 2], (1, 0, 2)).reshape(subnets, order)
    sources = jnp.concatenate(
        [amp_full * jnp.cos(angle_full)[:, None, :], amp_full * jnp.sin(angle_full)[:, None, :]], axis=1
    )
    sums = sums[:, : 7 * cases].reshape(subnets, 7, cases)
    denominator = sums[:, 6] + fault_res

    prod = fast("srj,scj->src", impedance, sources)
    prod_h = fast("srj,sjt->srt", impedance, h0_full)
    t0 = lax.iota(jnp.int32, steps)
    cw = jnp.asarray(np.cos(omega_step * np.arange(steps)), jnp.float32)
    sw = jnp.asarray(np.sin(omega_step * np.arange(steps)), jnp.float32)
    open0 = (
        cw[None, None, :, None] * prod[:, :, None, :cases]
        - sw[None, None, :, None] * prod[:, :, None, cases:]
        + prod_h[:, :, :, None]
    )
    fault0 = cw[None, :, None] * sums[:, 0][:, None] - sw[None, :, None] * sums[:, 1][:, None] + sums[:, 2 : 2 + steps]
    current0 = jnp.where(fault_step[:, None, :] <= t0[None, :, None], fault0 / denominator[:, None, :], 0.0)
    volt0 = open0 - current0[:, None] * fault_col[:, :, None, :]

    at_ends = pick("kn,nm->km", attach_map, volt0.reshape(local, steps * cases)).reshape(ends, steps, cases)
    waves = 2.0 * conductance[:, None, None] * at_ends - jnp.transpose(base[:steps])[:, :, None]

    slot_row = pair_slot[0]
    end_ids = lax.iota(jnp.int32, ends)
    selector = (end_ids[:, None] == slot_row[None, :]).astype(jnp.float32)
    selectorT = (slot_row[:, None] == end_ids[None, :]).astype(jnp.float32)
    outgoing = pick("pk,km->pm", selectorT, waves.reshape(ends, steps * cases))
    incoming = lax.all_to_all(outgoing, ("region", "node"), 0, 0, tiled=True)
    far = pick("kp,pm->km", selector, incoming).reshape(ends, steps, cases)

    taps_t = jnp.transpose(impulse_taps[:steps])
    base_t = jnp.transpose(base[steps:])
    hist_list = []
    for t in range(steps, total):
        history = base_t[:, t - steps][:, None]
        for j in range(t - steps + 1):
            history = history + taps_t[:, j][:, None] * far[:, t - steps - j]
        hist_list.append(history)
    hist1 = jnp.stack(hist_list, axis=1).reshape(ends, steps * cases)
    node_hist = pick("nk,km->nm", attach_mapT, hist1).reshape(subnets, rows, steps, cases)
    angle1 = jnp.asarray(omega_step * np.arange(steps, total), jnp.float32)
    phase = jnp.cos(angle1[None, None, :] + source_angle[:, :, None])
    inj1 = amp_t[:, :, None, :] * phase[:, :, :, None] + node_hist
    part1 = jnp.sum(fault_col[:, :, None, :] * inj1, axis=1)
    part1 = lax.all_to_all(jnp.broadcast_to(part1[None], (n_node,) + part1.shape), "node", 0, 0, tiled=True)
    sums1 = jnp.sum(part1, axis=0)
    gathered1 = lax.all_gather(inj1.reshape(subnets, rows, steps * cases), "node", axis=1, tiled=True)
    prod1 = fast("srj,sjm->srm", impedance, gathered1).reshape(subnets, rows, steps, cases)
    t1 = t0 + steps
    current1 = jnp.where(fault_step[:, None, :] <= t1[None, :, None], sums1 / denominator[:, None, :], 0.0)
    volt1 = prod1 - current1[:, None] * fault_col[:, :, None, :]
    volt = jnp.concatenate([volt0, volt1], axis=2)
    return jnp.transpose(volt, (2, 0, 3, 1))


def solution(mesh):
    in_specs = (
        P("region", "node", None),
        P("region", None, "node"),
        P("region", "node"),
        P(None, ("region", "node")),
        P(None, ("region", "node")),
        P(("region", "node")),
        P(("region", "node")),
        P(("region", "node"), None),
        P("region", None),
        P("region", None),
        P("region", None),
    )
    out_specs = P(None, "region", None, "node")
    return jax.shard_map(body, mesh=mesh, in_specs=in_specs, out_specs=out_specs, check_vma=False)
```
